512 devices in a mesh: leaf: 128 (over y, z, core), sub: 4 (over x).
Axes of the slice: x: 4, y: 8, z: 8, core: 2. Of those that a mesh axis runs over, the one named last changes fastest.
Arguments:
- probes: bfloat16 [32, 524288], P(None, ('leaf', 'sub')), may hold values from -6 to 6
- row_basis: bfloat16 [2048, 64, 256], P(('leaf', 'sub')), may hold values from -0.375 to 0.375
- col_basis: bfloat16 [2048, 64, 256], P(('leaf', 'sub')), may hold values from -0.75 to 0.75
- near_blocks: bfloat16 [2048, 5, 256, 256], P(('leaf', 'sub')), may hold values from -0.21875 to 0.21875
- near_cols: int32 [2048, 5], P(('leaf', 'sub')), may hold values from -1 to 2047, as said below
- far_leaf: int32 [2048, 4], P(('leaf', 'sub')), may hold values from -1 to 2047, as said below
- far_pair: int32 [1024, 4], P(('leaf', 'sub')), may hold values from -1 to 1023, as said below
- far_top: int32 [1020, 4], replicated, may hold values from -1 to 511, as said below
- row_transfer: float32 [9, 2, 64, 64], replicated, may hold values from -0.5 to 0.5
- col_transfer: float32 [9, 2, 64, 64], replicated, may hold values from -0.75 to 0.75
- coupling: float32 [10, 6, 64, 64], replicated, may hold values from -0.4375 to 0.4375
Outputs:
- result: float32 [32, 524288], P(None, ('leaf', 'sub'))
The draws below stay inside these ranges and needn't reach their ends.
Inputs may be any that keep to these rules, and one draw needn't show every extreme that they name: `near_cols`: slot j of leaf s holds s + j - 2 or -1; slot 2 always holds s. `far_leaf`: each entry of the row of box t is -1 or a child of a box beside t's parent, never t itself; a row's entries are distinct. `far_pair`: each entry of the row of box t is -1 or a child of a box beside t's parent, never t itself; a row's entries are distinct. `far_top`: rows of level 2 first, then level 3 and so on, boxes in order; entries are box numbers within their level, -1 or a child of a box beside the row box's parent, never the box itself, distinct within a row.
All inputs are finite; a program needn't handle non-finite values.
Results may differ from the reference program's by a relative error of at most 0.0028.
Values sent between devices are 32-bit elements; how exact they have to be, the bound alone decides.
No kernel may reach another device: no remote copies, remote signals or barrier semaphores. Data moves between devices by JAX's collectives and lax.ppermute only.
A program may use at most 128 MiB of HBM per device.

```python
import jax
import jax.numpy as jnp
from jax import lax

P_SIZE = 256
R = 64
PROBES = 32
LEAF_DEV = 4
NEAR = 5
LEVELS = 10
NLEAF = 2048
NPTS = 524288


def far_rows(key, box_count):
    box_ids = jnp.arange(box_count, dtype=jnp.int32)
    parents = box_ids // 2
    candidates = jnp.stack([2 * parents - 2, 2 * parents - 1, 2 * parents + 2, 2 * parents + 3], axis=1)
    rolls = jax.random.randint(key, (box_count, 4), 0, 4)
    inside = (candidates >= 0) & (candidates < box_count) & (rolls < 3)
    return jnp.where(inside, candidates, -1).astype(jnp.int32)


def draw_near_cols(key, part):
    rate_key, roll_key = jax.random.split(key)
    leaf_ids = jnp.arange(NLEAF, dtype=jnp.int32)
    owners = leaf_ids // LEAF_DEV
    rates = jax.random.randint(rate_key, (NLEAF // LEAF_DEV,), 0, 5)[owners]
    rolls = jax.random.randint(roll_key, (NLEAF, NEAR), 0, 4)
    shifts = jnp.arange(NEAR, dtype=jnp.int32) - NEAR // 2
    columns = leaf_ids[:, None] + shifts[None, :]
    keep = (rolls < rates[:, None]) | (shifts[None, :] == 0)
    inside = (columns >= 0) & (columns < NLEAF)
    return jnp.where(keep & inside, columns, -1).astype(jnp.int32)


def draw_far_leaf(key, part):
    return far_rows(jax.random.fold_in(key, 11), NLEAF)


def draw_far_pair(key, part):
    return far_rows(jax.random.fold_in(key, 12), NLEAF // 2)


def draw_far_top(key, part):
    pieces = []
    box_count = NLEAF // 4
    while box_count >= 4:
        pieces.append(far_rows(jax.random.fold_in(key, 100 + box_count), box_count))
        box_count = box_count // 2
    return jnp.concatenate(pieces, axis=0)


def shard_levels(rng, dims, cuts, least, largest):
    def one(position, blocks):
        heights = jax.random.uniform(jax.random.fold_in(jax.random.fold_in(rng, 6), position), (blocks,), jnp.float32, least / len(cuts), largest / len(cuts))
        return jnp.repeat(jnp.exp(heights), dims[position] // blocks).reshape((-1,) + (1,) * (len(dims) - position - 1))

    level = one(*cuts[0])
    for cut in cuts[1:]:
        level = level * one(*cut)
    return level


def normal_values(rng, extent, deviation, most, cuts=(), kind=jnp.bfloat16):
    result = deviation * jax.random.normal(rng, extent, jnp.float32)
    if cuts:
        result = result * shard_levels(rng, extent, cuts, -0.22, 0.18)
    return jnp.clip(result, -most, most).astype(kind)


def setup_inputs(seed: int = 0) -> dict:
    arg_keys = jax.random.split(jax.random.key(seed), 12)
    return {
        "probes": normal_values(arg_keys[0], (PROBES, NPTS), 1.0, 6.0, ((1, 512),)),
        "row_basis": normal_values(arg_keys[1], (NLEAF, R, P_SIZE), P_SIZE ** -0.5, 0.375, ((0, 512),)),
        "col_basis": normal_values(arg_keys[2], (NLEAF, R, P_SIZE), R ** -0.5, 0.75, ((0, 512),)),
        "near_blocks": normal_values(arg_keys[3], (NLEAF, NEAR, P_SIZE, P_SIZE), (3 * P_SIZE) ** -0.5, 0.21875, ((0, 512),)),
        "near_cols": draw_near_cols(jax.random.fold_in(arg_keys[11], 71), 0),
        "far_leaf": draw_far_leaf(jax.random.fold_in(arg_keys[11], 71), 0),
        "far_pair": draw_far_pair(jax.random.fold_in(arg_keys[11], 71), 0),
        "far_top": draw_far_top(jax.random.fold_in(arg_keys[11], 71), 0),
        "row_transfer": normal_values(arg_keys[8], (LEVELS - 1, 2, R, R), (2 * R) ** -0.5, 0.5, (), jnp.float32),
        "col_transfer": normal_values(arg_keys[9], (LEVELS - 1, 2, R, R), R ** -0.5, 0.75, (), jnp.float32),
        "coupling": normal_values(arg_keys[10], (LEVELS, 6, R, R), (3 * R) ** -0.5, 0.4375, (), jnp.float32),
    }


highest = lax.Precision.HIGHEST


def couple_level(coefficients, list_rows, level_coupling):
    box_total = list_rows.shape[0]
    usable = list_rows >= 0
    source = jnp.where(usable, list_rows, 0).astype(jnp.int32)
    offset = source - jnp.arange(box_total, dtype=jnp.int32)[:, None]
    class_ids = jnp.where(usable, offset + 3 - (offset > 0).astype(jnp.int32), 0).astype(jnp.int32)
    picked = coefficients[source] * usable[:, :, None, None].astype(jnp.float32)
    matrices = level_coupling[class_ids]
    return jnp.einsum('bjkr,bjrs->bks', picked, matrices, precision=highest)


def leaf_products(item):
    leaf_points, blocks = item
    return jnp.einsum('kp,jpq->jkq', leaf_points, blocks.astype(jnp.float32), precision=highest)


def reference(probes, row_basis, col_basis, near_blocks, near_cols, far_leaf, far_pair, far_top, row_transfer, col_transfer, coupling):
    leaves = NLEAF
    points = jnp.transpose(probes.reshape(PROBES, leaves, P_SIZE), (1, 0, 2)).astype(jnp.float32)
    upward = [jnp.einsum('lkp,lrp->lkr', points, row_basis.astype(jnp.float32), precision=highest)]
    for height in range(LEVELS - 1):
        paired = upward[-1].reshape(-1, 2, PROBES, R)
        from_even = jnp.einsum('bkr,rs->bks', paired[:, 0], row_transfer[height, 0], precision=highest)
        from_odd = jnp.einsum('bkr,rs->bks', paired[:, 1], row_transfer[height, 1], precision=highest)
        upward.append(from_even + from_odd)
    lists = [far_leaf, far_pair]
    row_start = 0
    for height in range(2, LEVELS):
        box_total = leaves >> height
        lists.append(far_top[row_start:row_start + box_total])
        row_start = row_start + box_total
    expansion = couple_level(upward[LEVELS - 1], lists[LEVELS - 1], coupling[LEVELS - 1])
    for height in range(LEVELS - 2, -1, -1):
        from_even = jnp.einsum('bkr,rs->bks', expansion, col_transfer[height, 0], precision=highest)
        from_odd = jnp.einsum('bkr,rs->bks', expansion, col_transfer[height, 1], precision=highest)
        pushed = jnp.stack([from_even, from_odd], axis=1).reshape(-1, PROBES, R)
        expansion = pushed + couple_level(upward[height], lists[height], coupling[height])
    leaf_field = expansion.astype(jnp.bfloat16)
    far_field = jnp.einsum('lkr,lrp->lkp', leaf_field.astype(jnp.float32), col_basis.astype(jnp.float32), precision=highest)
    products = lax.map(leaf_products, (points, near_blocks))
    targets = jnp.where(near_cols >= 0, near_cols, leaves).astype(jnp.int32).reshape(-1)
    near_field = jax.ops.segment_sum(products.reshape(-1, PROBES, P_SIZE), targets, num_segments=leaves + 1)[:leaves]
    total = far_field + near_field
    return jnp.transpose(total, (1, 0, 2)).reshape(PROBES, leaves * P_SIZE)
```

```python
import jax
import jax.numpy as jnp
from jax import lax
from jax.sharding import Mesh
from jax.sharding import PartitionSpec as P

highest = lax.Precision.HIGHEST
ALL = ("yz", "core", "sub")
GROUP = ("core", "sub")


def padded(shard, axis, width):
    devices, length = (lax.axis_size(axis), shard.shape[0])
    up = [(i, i + 1) for i in range(devices - 1)]
    down = [(j, i) for i, j in up]
    before = lax.ppermute(shard[length - width :], axis, up)
    after = lax.ppermute(shard[:width], axis, down)
    return jnp.concatenate([before, shard, after], axis=0)


def halve(coefficients, transfer):
    paired = coefficients.reshape(
        coefficients.shape[0] // 2, 2, coefficients.shape[1], coefficients.shape[2]
    )
    return jnp.einsum("bjkr,jrs->bks", paired, transfer, precision=highest)


def window_coupling(windows, bases, rows, odd, level_coupling):
    picks = (0, 1, 4, 5)
    stacked = jnp.concatenate([windows[:, w] for w in picks], axis=-1)
    hits = [
        jnp.any((rows == (bases + w)[:, None]) & (rows >= 0), axis=1) for w in picks
    ]
    even_cls = (1, 2, 4, 5)
    odd_cls = (0, 1, 3, 4)
    mats = []
    for i in range(4):
        chosen = jnp.where(
            odd[:, None, None], level_coupling[odd_cls[i]], level_coupling[even_cls[i]]
        )
        mats.append(jnp.where(hits[i][:, None, None], chosen, 0.0))
    matrix = jnp.concatenate(mats, axis=1)
    return jnp.einsum("bkr,brs->bks", stacked, matrix, precision=highest)


def one_box(level_array, offset, box, row, level_coupling):
    base = 2 * (box >> 1) - 2
    win = lax.dynamic_slice_in_dim(level_array, base - offset, 6, axis=0)
    return window_coupling(
        win[None], jnp.reshape(base, (1,)), row[None], jnp.reshape(box & 1, (1,)) == 1,
        level_coupling,
    )[0]


def local(
    probes,
    row_basis,
    col_basis,
    near_blocks,
    near_cols,
    far_leaf,
    far_pair,
    far_top,
    row_transfer,
    col_transfer,
    coupling,
):
    leaves, basis_rank, leaf_width = row_basis.shape
    probe_count = probes.shape[0]
    near_reach = near_cols.shape[1] // 2
    levels_total = coupling.shape[0]
    devices = lax.axis_size(ALL)
    device = lax.axis_index(ALL)
    group_size = lax.axis_size(GROUP)
    in_group = lax.axis_index(GROUP)
    group = lax.axis_index("yz")
    groups = lax.axis_size("yz")
    all_leaves = devices * leaves
    first_leaf = device * leaves
    points = probes.reshape(probe_count, leaves, leaf_width)

    a0 = jnp.einsum("klp,lrp->lkr", points, row_basis, preferred_element_type=jnp.float32)
    a1 = halve(a0, row_transfer[0])
    a2 = halve(a1, row_transfer[1])

    grp = lax.all_gather(a2[0], GROUP, axis=0, tiled=False)
    up_levels = [grp]
    for height in range(2, 5):
        up_levels.append(halve(up_levels[-1], row_transfer[height]))
    own5 = up_levels[-1]
    top = [lax.all_gather(own5[0], "yz", axis=0, tiled=False)]
    for height in range(5, levels_total - 1):
        top.append(halve(top[-1], row_transfer[height]))

    ext = [padded(grp, "yz", group_size)]
    for height in range(2, 4):
        ext.append(halve(ext[-1], row_transfer[height]))

    products = jnp.einsum("klp,ljpq->ljkq", points, near_blocks, preferred_element_type=jnp.float32)
    span_width = leaves + 2 * near_reach
    targets = near_cols - (first_leaf - near_reach)
    places = jnp.arange(span_width, dtype=jnp.int32)
    scatter_table = (
        (targets[:, :, None] == places[None, None, :]) & (near_cols >= 0)[:, :, None]
    ).astype(jnp.float32)
    spread = jnp.einsum("lje,ljkq->ekq", scatter_table, products, precision=highest)
    rims = jnp.concatenate([spread[:near_reach], spread[span_width - near_reach :]], axis=0)
    rim_ext = padded(rims, ALL, near_reach)
    own_near = spread[near_reach : near_reach + leaves]
    own_near = own_near.at[:near_reach].add(rim_ext[:near_reach])
    own_near = own_near.at[leaves - near_reach :].add(rim_ext[3 * near_reach :])

    packed = jnp.concatenate([a0, a1], axis=0)
    pack_ext = padded(packed, ALL, packed.shape[0])
    rows_pack = packed.shape[0]
    ext0 = jnp.concatenate(
        [pack_ext[:leaves], a0, pack_ext[rows_pack + rows_pack : rows_pack * 2 + leaves]], axis=0
    )
    ext1 = jnp.concatenate(
        [pack_ext[leaves:rows_pack], a1, pack_ext[rows_pack * 2 + leaves :]], axis=0
    )

    starts = {}
    running = 0
    for height in range(2, levels_total):
        starts[height] = running
        running = running + (all_leaves >> height)

    def top_row(height, box):
        return lax.dynamic_index_in_dim(far_top, starts[height] + box, 0, keepdims=False)

    g = {}
    for height in range(5, levels_total):
        arr = top[height - 5]
        arr = jnp.pad(arr, ((2, 2), (0, 0), (0, 0)))
        box = group >> (height - 5)
        g[height] = one_box(arr, -2, box, top_row(height, box), coupling[height])
    for height in range(2, 5):
        arr = ext[height - 2]
        box = device >> (height - 2)
        offset = (group - 1) * (group_size >> (height - 2))
        g[height] = one_box(arr, offset, box, top_row(height, box), coupling[height])

    expansion = g[levels_total - 1]
    for height in range(levels_total - 2, 1, -1):
        box = device >> (height - 2)
        matrix = lax.dynamic_index_in_dim(col_transfer[height], box & 1, 0, keepdims=False)
        expansion = g[height] + jnp.dot(expansion, matrix, precision=highest)

    odd1 = jnp.array([False, True])
    bases1 = jnp.full((2,), 2 * device - 2, jnp.int32)
    win1 = jnp.stack([ext1[0:6], ext1[0:6]], axis=0)
    g1 = window_coupling(win1, bases1, far_pair, odd1, coupling[1])
    b1 = jnp.einsum("kr,jrs->jks", expansion, col_transfer[1], precision=highest) + g1

    odd0 = jnp.array([False, True, False, True])
    local_starts = (2, 2, 4, 4)
    bases0 = first_leaf + jnp.array([0, 0, 2, 2], jnp.int32) - 2
    win0 = jnp.stack([ext0[s : s + 6] for s in local_starts], axis=0)
    g0 = window_coupling(win0, bases0, far_leaf, odd0, coupling[0])
    pushed = jnp.einsum("jkr,crs->jcks", b1, col_transfer[0], precision=highest)
    b0 = pushed.reshape(leaves, probe_count, basis_rank) + g0

    far_field = jnp.einsum(
        "lkr,lrp->klp",
        b0.astype(jnp.bfloat16),
        col_basis,
        preferred_element_type=jnp.float32,
    )
    own_near_t = jnp.transpose(own_near, (1, 0, 2))
    return (far_field + own_near_t).reshape(probe_count, leaves * leaf_width)


def solution(mesh):
    leaf_count, sub_count = mesh.devices.shape
    fine = Mesh(mesh.devices.reshape(leaf_count // 2, 2, sub_count), ALL)
    in_specs = (
        P(None, ALL),
        P(ALL, None, None),
        P(ALL, None, None),
        P(ALL, None, None, None),
        P(ALL, None),
        P(ALL, None),
        P(ALL, None),
        P(),
        P(),
        P(),
        P(),
    )
    out_specs = P(None, ALL)
    return jax.shard_map(local, mesh=fine, in_specs=in_specs, out_specs=out_specs, check_vma=False)
```

```python
import jax
import jax.numpy as jnp
from jax import lax
from jax.sharding import Mesh
from jax.sharding import PartitionSpec as P

highest = lax.Precision.HIGHEST
ALL = ("yz", "core", "sub")
GROUP = ("core", "sub")


def padded(shard, axis, width):
    devices, length = (lax.axis_size(axis), shard.shape[0])
    up = [(i, i + 1) for i in range(devices - 1)]
    down = [(j, i) for i, j in up]
    before = lax.ppermute(shard[length - width :], axis, up)
    after = lax.ppermute(shard[:width], axis, down)
    return jnp.concatenate([before, shard, after], axis=0)


def halve(coefficients, transfer):
    paired = coefficients.reshape(
        coefficients.shape[0] // 2, 2, coefficients.shape[1], coefficients.shape[2]
    )
    return jnp.einsum("bjkr,jrs->bks", paired, transfer, precision=highest)


def class_blocks(windows, bases, rows, odd):
    masked = []
    for w in (0, 1, 4, 5):
        hit = jnp.any((rows == (bases + w)[:, None]) & (rows >= 0), axis=1)
        masked.append(jnp.where(hit[:, None, None], windows[:, w], 0.0))
    zero = jnp.zeros_like(masked[0])
    m0, m1, m4, m5 = masked
    odd_blocks = jnp.concatenate([m0, m1, zero, m4, m5, zero], axis=-1)
    even_blocks = jnp.concatenate([zero, m0, m1, zero, m4, m5], axis=-1)
    return jnp.where(odd[:, None, None], odd_blocks, even_blocks)


def one_box(level_array, offset, box, row):
    base = 2 * (box >> 1) - 2
    win = lax.dynamic_slice_in_dim(level_array, base - offset, 6, axis=0)
    return class_blocks(
        win[None], jnp.reshape(base, (1,)), row[None], jnp.reshape(box & 1, (1,)) == 1
    )[0]


def local(
    probes,
    row_basis,
    col_basis,
    near_blocks,
    near_cols,
    far_leaf,
    far_pair,
    far_top,
    row_transfer,
    col_transfer,
    coupling,
):
    leaves, basis_rank, leaf_width = row_basis.shape
    probe_count = probes.shape[0]
    near_reach = near_cols.shape[1] // 2
    levels_total = coupling.shape[0]
    devices = lax.axis_size(ALL)
    device = lax.axis_index(ALL)
    group_size = lax.axis_size(GROUP)
    in_group = lax.axis_index(GROUP)
    group = lax.axis_index("yz")
    groups = lax.axis_size("yz")
    all_leaves = devices * leaves
    first_leaf = device * leaves
    points = probes.reshape(probe_count, leaves, leaf_width)

    a0 = jnp.einsum("klp,lrp->lkr", points, row_basis, preferred_element_type=jnp.float32)
    a1 = halve(a0, row_transfer[0])
    a2 = halve(a1, row_transfer[1])

    slot = jnp.arange(group_size, dtype=jnp.int32) == in_group
    grp = lax.psum(jnp.where(slot[:, None, None], a2, 0.0), GROUP)
    share = a2[0]
    for height in range(2, 5):
        bit = (device >> (height - 2)) & 1
        matrix = row_transfer[height].reshape(2 * basis_rank, basis_rank)
        share = jnp.dot(
            jnp.concatenate([jnp.where(bit == 0, share, 0.0), jnp.where(bit == 1, share, 0.0)], axis=-1),
            matrix,
            precision=highest,
        )
    gslot = jnp.arange(groups, dtype=jnp.int32) == group
    top = [lax.psum(jnp.where(gslot[:, None, None], share[None], 0.0), ALL)]
    for height in range(5, levels_total - 1):
        top.append(halve(top[-1], row_transfer[height]))

    ext = [padded(grp, "yz", group_size)]
    for height in range(2, 4):
        ext.append(halve(ext[-1], row_transfer[height]))

    products = jnp.einsum("klp,ljpq->ljkq", points, near_blocks, preferred_element_type=jnp.float32)
    span_width = leaves + 2 * near_reach
    targets = near_cols - (first_leaf - near_reach)
    places = jnp.arange(span_width, dtype=jnp.int32)
    scatter_table = (
        (targets[:, :, None] == places[None, None, :]) & (near_cols >= 0)[:, :, None]
    ).astype(jnp.float32)
    spread = jnp.einsum("lje,ljkq->ekq", scatter_table, products, precision=highest)
    rims = jnp.concatenate([spread[:near_reach], spread[span_width - near_reach :]], axis=0)
    rim_ext = padded(rims, ALL, near_reach)
    own_near = spread[near_reach : near_reach + leaves]
    own_near = own_near.at[:near_reach].add(rim_ext[:near_reach])
    own_near = own_near.at[leaves - near_reach :].add(rim_ext[3 * near_reach :])

    packed = jnp.concatenate([a0, a1], axis=0)
    pack_ext = padded(packed, ALL, packed.shape[0])
    rows_pack = packed.shape[0]
    ext0 = jnp.concatenate(
        [pack_ext[:leaves], a0, pack_ext[rows_pack + rows_pack : rows_pack * 2 + leaves]], axis=0
    )
    ext1 = jnp.concatenate(
        [pack_ext[leaves:rows_pack], a1, pack_ext[rows_pack * 2 + leaves :]], axis=0
    )

    starts = {}
    running = 0
    for height in range(2, levels_total):
        starts[height] = running
        running = running + (all_leaves >> height)

    def top_row(height, box):
        return lax.dynamic_index_in_dim(far_top, starts[height] + box, 0, keepdims=False)

    blocks_top = []
    for height in range(5, levels_total):
        arr = jnp.pad(top[height - 5], ((2, 2), (0, 0), (0, 0)))
        box = group >> (height - 5)
        blocks_top.append(one_box(arr, -2, box, top_row(height, box)))
    cpl = coupling.reshape(levels_total, 6 * basis_rank, basis_rank)
    g_top = jnp.einsum("lkc,lcs->lks", jnp.stack(blocks_top), cpl[5:], precision=highest)
    blocks_mid = []
    for height in range(2, 5):
        box = device >> (height - 2)
        offset = (group - 1) * (group_size >> (height - 2))
        blocks_mid.append(one_box(ext[height - 2], offset, box, top_row(height, box)))
    g_mid = jnp.einsum("lkc,lcs->lks", jnp.stack(blocks_mid), cpl[2:5], precision=highest)
    g = {height: g_top[height - 5] for height in range(5, levels_total)}
    g.update({height: g_mid[height - 2] for height in range(2, 5)})

    expansion = g[levels_total - 1]
    for height in range(levels_total - 2, 1, -1):
        bit = (device >> (height - 2)) & 1
        matrix = col_transfer[height].reshape(2 * basis_rank, basis_rank)
        spread_b = jnp.concatenate(
            [jnp.where(bit == 0, expansion, 0.0), jnp.where(bit == 1, expansion, 0.0)], axis=-1
        )
        expansion = g[height] + jnp.dot(spread_b, matrix, precision=highest)

    odd1 = jnp.array([False, True])
    bases1 = jnp.full((2,), 2 * device - 2, jnp.int32)
    win1 = jnp.stack([ext1[0:6], ext1[0:6]], axis=0)
    g1 = jnp.einsum(
        "bkc,cs->bks", class_blocks(win1, bases1, far_pair, odd1), cpl[1], precision=highest
    )
    b1 = jnp.einsum("kr,jrs->jks", expansion, col_transfer[1], precision=highest) + g1

    odd0 = jnp.array([False, True, False, True])
    local_starts = (2, 2, 4, 4)
    bases0 = first_leaf + jnp.array([0, 0, 2, 2], jnp.int32) - 2
    win0 = jnp.stack([ext0[st : st + 6] for st in local_starts], axis=0)
    g0 = jnp.einsum(
        "bkc,cs->bks", class_blocks(win0, bases0, far_leaf, odd0), cpl[0], precision=highest
    )
    pushed = jnp.einsum("jkr,crs->jcks", b1, col_transfer[0], precision=highest)
    b0 = pushed.reshape(leaves, probe_count, basis_rank) + g0

    far_field = jnp.einsum(
        "lkr,lrp->klp",
        b0.astype(jnp.bfloat16),
        col_basis,
        preferred_element_type=jnp.float32,
    )
    own_near_t = jnp.transpose(own_near, (1, 0, 2))
    return (far_field + own_near_t).reshape(probe_count, leaves * leaf_width)


def solution(mesh):
    leaf_count, sub_count = mesh.devices.shape
    fine = Mesh(mesh.devices.reshape(leaf_count // 2, 2, sub_count), ALL)
    in_specs = (
        P(None, ALL),
        P(ALL, None, None),
        P(ALL, None, None),
        P(ALL, None, None, None),
        P(ALL, None),
        P(ALL, None),
        P(ALL, None),
        P(),
        P(),
        P(),
        P(),
    )
    out_specs = P(None, ALL)
    return jax.shard_map(local, mesh=fine, in_specs=in_specs, out_specs=out_specs, check_vma=False)
```

```python
import functools

import jax
import jax.numpy as jnp
from jax import lax
from jax.sharding import Mesh
from jax.experimental import pallas as pl
from jax.experimental.pallas import tpu as pltpu
from jax.sharding import PartitionSpec as P

highest = lax.Precision.HIGHEST
ALL = ("yz", "core", "sub")
GROUP = ("core", "sub")


def padded(shard, axis, width):
    devices, length = (lax.axis_size(axis), shard.shape[0])
    up = [(i, i + 1) for i in range(devices - 1)]
    down = [(j, i) for i, j in up]
    before = lax.ppermute(shard[length - width :], axis, up)
    after = lax.ppermute(shard[:width], axis, down)
    return jnp.concatenate([before, shard, after], axis=0)


def halve(coefficients, transfer):
    paired = coefficients.reshape(
        coefficients.shape[0] // 2, 2, coefficients.shape[1], coefficients.shape[2]
    )
    return jnp.einsum("bjkr,jrs->bks", paired, transfer, precision=highest)


def window_coupling(windows, bases, rows, odd, level_coupling):
    picks = (0, 1, 4, 5)
    stacked = jnp.concatenate([windows[:, w] for w in picks], axis=-1)
    hits = [
        jnp.any((rows == (bases + w)[:, None]) & (rows >= 0), axis=1) for w in picks
    ]
    even_cls = (1, 2, 4, 5)
    odd_cls = (0, 1, 3, 4)
    mats = []
    for i in range(4):
        chosen = jnp.where(
            odd[:, None, None], level_coupling[odd_cls[i]], level_coupling[even_cls[i]]
        )
        mats.append(jnp.where(hits[i][:, None, None], chosen, 0.0))
    matrix = jnp.concatenate(mats, axis=1)
    return jnp.einsum("bkr,brs->bks", stacked, matrix, precision=highest)


def one_box(level_array, offset, box, row, level_coupling):
    base = 2 * (box >> 1) - 2
    win = lax.dynamic_slice_in_dim(level_array, base - offset, 6, axis=0)
    return window_coupling(
        win[None], jnp.reshape(base, (1,)), row[None], jnp.reshape(box & 1, (1,)) == 1,
        level_coupling,
    )[0]


def tree_kernel(dev_ref, ftop_ref, fleaf_ref, fpair_ref, top5_ref, ext2_ref, ext0_ref, ext1_ref,
                rt_ref, ct_ref, cp_ref, cb_ref, near_ref, out_ref,
                p5, p6, p7, p8, p9, e3, e4, *, starts, k, r, leaves, width, levels):
    def dot(a, b):
        return jnp.dot(a, b, precision=highest, preferred_element_type=jnp.float32)

    def halve_rows(x, n, height):
        v = x.reshape(n // 2, 2 * k, r)
        even = v[:, :k].reshape(n // 2 * k, r)
        odd = v[:, k:].reshape(n // 2 * k, r)
        return dot(even, rt_ref[2 * height]) + dot(odd, rt_ref[2 * height + 1])

    def box(ref, i):
        return ref[pl.ds(pl.multiple_of(i * k, k), k), :]

    def coupling(ref, start, base, odd, row_at, level):
        total = jnp.zeros((k, r), jnp.float32)
        for w, cls in ((0, 1), (1, 2), (4, 4), (5, 5)):
            hit = jnp.int32(0)
            for j in range(4):
                e = row_at(j)
                hit = hit | ((e == base + w) & (e >= 0)).astype(jnp.int32)
            scale = hit.astype(jnp.float32)
            c = cls - odd
            total = total + dot(box(ref, start + w) * scale, cp_ref[level * 6 + c])
        return total

    d = dev_ref[0]
    grp = d >> 3
    zeros2 = jnp.zeros((2 * k, r), jnp.float32)
    pads = [p5, p6, p7, p8, p9]
    x = top5_ref[...]
    n = x.shape[0] // k
    for idx, ref in enumerate(pads):
        ref[pl.ds(0, 2 * k), :] = zeros2
        ref[pl.ds((n + 2) * k, 2 * k), :] = zeros2
        ref[pl.ds(2 * k, n * k), :] = x
        if idx + 1 < len(pads):
            x = halve_rows(x, n, 5 + idx)
            n = n // 2
    e3[...] = halve_rows(ext2_ref[...], 24, 2)
    e4[...] = halve_rows(e3[...], 12, 3)

    g = {}
    for height in range(5, levels):
        t = grp >> (height - 5)
        base = 2 * (t >> 1) - 2
        row0 = (starts[height] + t) * 4
        g[height] = coupling(pads[height - 5], base + 2, base, t & 1,
                             lambda j, row0=row0: ftop_ref[row0 + j], height)
    lg = d & 7
    mids = {2: (ext2_ref, 2 * (lg >> 1) + 6), 3: (e3, 2 * (lg >> 2) + 2), 4: (e4, 0)}
    for height in range(2, 5):
        t = d >> (height - 2)
        base = 2 * (t >> 1) - 2
        row0 = (starts[height] + t) * 4
        ref, start = mids[height]
        g[height] = coupling(ref, start, base, t & 1,
                             lambda j, row0=row0: ftop_ref[row0 + j], height)
    expansion = g[levels - 1]
    for height in range(levels - 2, 1, -1):
        bit = (d >> (height - 2)) & 1
        expansion = g[height] + dot(expansion, ct_ref[2 * height + bit])
    b1 = []
    for j in range(2):
        gj = coupling(ext1_ref, 0, 2 * d - 2, j, lambda e, j=j: fpair_ref[j * 4 + e], 1)
        b1.append(gj + dot(expansion, ct_ref[2 + j]))
    for i in range(leaves):
        st = 2 * (i >> 1) + 2
        gi = coupling(ext0_ref, st, leaves * d + 2 * (i >> 1) - 2, i & 1,
                      lambda e, i=i: fleaf_ref[i * 4 + e], 0)
        b0 = gi + dot(b1[i >> 1], ct_ref[i & 1])
        far = jnp.dot(b0.astype(jnp.bfloat16), cb_ref[i], preferred_element_type=jnp.float32)
        out_ref[:, pl.ds(i * width, width)] = far + near_ref[i]


def local(
    probes,
    row_basis,
    col_basis,
    near_blocks,
    near_cols,
    far_leaf,
    far_pair,
    far_top,
    row_transfer,
    col_transfer,
    coupling,
):
    leaves, basis_rank, leaf_width = row_basis.shape
    probe_count = probes.shape[0]
    near_reach = near_cols.shape[1] // 2
    levels_total = coupling.shape[0]
    devices = lax.axis_size(ALL)
    device = lax.axis_index(ALL)
    group_size = lax.axis_size(GROUP)
    in_group = lax.axis_index(GROUP)
    group = lax.axis_index("yz")
    groups = lax.axis_size("yz")
    all_leaves = devices * leaves
    first_leaf = device * leaves
    points = probes.reshape(probe_count, leaves, leaf_width)

    a0 = jnp.einsum("klp,lrp->lkr", points, row_basis, preferred_element_type=jnp.float32)
    a1 = halve(a0, row_transfer[0])
    a2 = halve(a1, row_transfer[1])

    grp = lax.all_gather(a2[0], GROUP, axis=0, tiled=False)
    up_levels = [grp]
    for height in range(2, 5):
        up_levels.append(halve(up_levels[-1], row_transfer[height]))

    products = jnp.einsum("klp,ljpq->ljkq", points, near_blocks, preferred_element_type=jnp.float32)
    span_width = leaves + 2 * near_reach
    targets = near_cols - (first_leaf - near_reach)
    places = jnp.arange(span_width, dtype=jnp.int32)
    scatter_table = (
        (targets[:, :, None] == places[None, None, :]) & (near_cols >= 0)[:, :, None]
    ).astype(jnp.float32)
    spread = jnp.einsum("lje,ljkq->ekq", scatter_table, products, precision=highest)
    rims = jnp.concatenate([spread[:near_reach], spread[span_width - near_reach :]], axis=0)
    rim_ext = padded(rims, ALL, near_reach)
    own_near = spread[near_reach : near_reach + leaves]
    own_near = own_near.at[:near_reach].add(rim_ext[:near_reach])
    own_near = own_near.at[leaves - near_reach :].add(rim_ext[3 * near_reach :])

    packed = jnp.concatenate([a0, a1], axis=0)
    pack_ext = padded(packed, ALL, packed.shape[0])
    rows_pack = packed.shape[0]
    ext0 = jnp.concatenate(
        [pack_ext[:leaves], a0, pack_ext[rows_pack + rows_pack : rows_pack * 2 + leaves]], axis=0
    )
    ext1 = jnp.concatenate(
        [pack_ext[leaves:rows_pack], a1, pack_ext[rows_pack * 2 + leaves :]], axis=0
    )

    starts = {}
    running = 0
    for height in range(2, levels_total):
        starts[height] = running
        running = running + (all_leaves >> height)

    gathered = lax.all_gather(up_levels[-1][0], "yz", axis=0, tiled=False)
    ext2 = padded(grp, "yz", group_size)
    k, r = probe_count, basis_rank
    flat = lambda x: x.reshape(-1, r)
    n5 = gathered.shape[0]
    smem = pl.BlockSpec(memory_space=pltpu.SMEM)
    vmem = pl.BlockSpec(memory_space=pltpu.VMEM)
    out = pl.pallas_call(
        functools.partial(tree_kernel, starts=starts, k=k, r=r, leaves=leaves,
                          width=leaf_width, levels=levels_total),
        out_shape=jax.ShapeDtypeStruct((probe_count, leaves * leaf_width), jnp.float32),
        in_specs=[smem] * 4 + [vmem] * 9,
        out_specs=vmem,
        scratch_shapes=[pltpu.VMEM(((n5 >> i) * k + 4 * k, r), jnp.float32) for i in range(5)]
        + [pltpu.VMEM((12 * k, r), jnp.float32), pltpu.VMEM((6 * k, r), jnp.float32)],
    )(
        jnp.reshape(device, (1,)).astype(jnp.int32),
        far_top.reshape(-1),
        far_leaf.reshape(-1),
        far_pair.reshape(-1),
        flat(gathered),
        flat(ext2),
        flat(ext0),
        flat(ext1),
        row_transfer.reshape(-1, r, r),
        col_transfer.reshape(-1, r, r),
        coupling.reshape(-1, r, r),
        col_basis,
        own_near,
    )
    return out


def solution(mesh):
    leaf_count, sub_count = mesh.devices.shape
    fine = Mesh(mesh.devices.reshape(leaf_count // 2, 2, sub_count), ALL)
    in_specs = (
        P(None, ALL),
        P(ALL, None, None),
        P(ALL, None, None),
        P(ALL, None, None, None),
        P(ALL, None),
        P(ALL, None),
        P(ALL, None),
        P(),
        P(),
        P(),
        P(),
    )
    out_specs = P(None, ALL)
    return jax.shard_map(local, mesh=fine, in_specs=in_specs, out_specs=out_specs, check_vma=False)
```

```python
import functools

import jax
import jax.numpy as jnp
from jax import lax
from jax.sharding import Mesh
from jax.experimental import pallas as pl
from jax.experimental.pallas import tpu as pltpu
from jax.sharding import PartitionSpec as P

highest = lax.Precision.HIGHEST
ALL = ("yz", "core", "sub")
GROUP = ("core", "sub")


def padded(shard, axis, width):
    devices, length = (lax.axis_size(axis), shard.shape[0])
    up = [(i, i + 1) for i in range(devices - 1)]
    down = [(j, i) for i, j in up]
    before = lax.ppermute(shard[length - width :], axis, up)
    after = lax.ppermute(shard[:width], axis, down)
    return before, after


def halve(coefficients, transfer):
    paired = coefficients.reshape(
        coefficients.shape[0] // 2, 2, coefficients.shape[1], coefficients.shape[2]
    )
    return jnp.einsum("bjkr,jrs->bks", paired, transfer, precision=highest)


def window_coupling(windows, bases, rows, odd, level_coupling):
    picks = (0, 1, 4, 5)
    stacked = jnp.concatenate([windows[:, w] for w in picks], axis=-1)
    hits = [
        jnp.any((rows == (bases + w)[:, None]) & (rows >= 0), axis=1) for w in picks
    ]
    even_cls = (1, 2, 4, 5)
    odd_cls = (0, 1, 3, 4)
    mats = []
    for i in range(4):
        chosen = jnp.where(
            odd[:, None, None], level_coupling[odd_cls[i]], level_coupling[even_cls[i]]
        )
        mats.append(jnp.where(hits[i][:, None, None], chosen, 0.0))
    matrix = jnp.concatenate(mats, axis=1)
    return jnp.einsum("bkr,brs->bks", stacked, matrix, precision=highest)


def one_box(level_array, offset, box, row, level_coupling):
    base = 2 * (box >> 1) - 2
    win = lax.dynamic_slice_in_dim(level_array, base - offset, 6, axis=0)
    return window_coupling(
        win[None], jnp.reshape(base, (1,)), row[None], jnp.reshape(box & 1, (1,)) == 1,
        level_coupling,
    )[0]


def tree_kernel(dev_ref, ftop_ref, fleaf_ref, fpair_ref, top5_ref, gb_ref, gown_ref, ga_ref,
                pb_ref, pown_ref, pa_ref, rt_ref, ct_ref, cp_ref, cb_ref, spread_ref, rb_ref, ra_ref,
                out_ref, p5, p6, p7, p8, p9, ext2_ref, e3, e4, *, starts, k, r, leaves, width, levels,
                reach):
    def dot(a, b):
        return jnp.dot(a, b, precision=highest, preferred_element_type=jnp.float32)

    def halve_rows(x, n, height):
        v = x.reshape(n // 2, 2 * k, r)
        even = v[:, :k].reshape(n // 2 * k, r)
        odd = v[:, k:].reshape(n // 2 * k, r)
        return dot(even, rt_ref[2 * height]) + dot(odd, rt_ref[2 * height + 1])

    def box(ref, i):
        return ref[pl.ds(pl.multiple_of(i * k, k), k), :]

    def coupling(get, base, odd, row_at, level):
        total = jnp.zeros((k, r), jnp.float32)
        for w, cls in ((0, 1), (1, 2), (4, 4), (5, 5)):
            hit = jnp.int32(0)
            for j in range(4):
                e = row_at(j)
                hit = hit | ((e == base + w) & (e >= 0)).astype(jnp.int32)
            scale = hit.astype(jnp.float32)
            c = cls - odd
            total = total + dot(get(w) * scale, cp_ref[level * 6 + c])
        return total

    d = dev_ref[0]
    grp = d >> 3
    zeros2 = jnp.zeros((2 * k, r), jnp.float32)
    pads = [p5, p6, p7, p8, p9]
    x = top5_ref[...]
    n = x.shape[0] // k
    for idx, ref in enumerate(pads):
        ref[pl.ds(0, 2 * k), :] = zeros2
        ref[pl.ds((n + 2) * k, 2 * k), :] = zeros2
        ref[pl.ds(2 * k, n * k), :] = x
        if idx + 1 < len(pads):
            x = halve_rows(x, n, 5 + idx)
            n = n // 2
    span = gown_ref.shape[0]
    ext2_ref[pl.ds(0, span), :] = gb_ref[...]
    ext2_ref[pl.ds(span, span), :] = gown_ref[...]
    ext2_ref[pl.ds(2 * span, span), :] = ga_ref[...]
    e3[...] = halve_rows(ext2_ref[...], 24, 2)
    e4[...] = halve_rows(e3[...], 12, 3)

    g = {}
    for height in range(5, levels):
        t = grp >> (height - 5)
        base = 2 * (t >> 1) - 2
        row0 = starts[height] + t
        g[height] = coupling(lambda w, ref=pads[height - 5], st=base + 2: box(ref, st + w),
                             base, t & 1, lambda j, row=row0: ftop_ref[row, j], height)
    lg = d & 7
    mids = {2: (ext2_ref, 2 * (lg >> 1) + 6), 3: (e3, 2 * (lg >> 2) + 2), 4: (e4, 0)}
    for height in range(2, 5):
        t = d >> (height - 2)
        base = 2 * (t >> 1) - 2
        row0 = starts[height] + t
        ref, start = mids[height]
        g[height] = coupling(lambda w, ref=ref, st=start: box(ref, st + w),
                             base, t & 1, lambda j, row=row0: ftop_ref[row, j], height)
    expansion = g[levels - 1]
    for height in range(levels - 2, 1, -1):
        bit = (d >> (height - 2)) & 1
        expansion = g[height] + dot(expansion, ct_ref[2 * height + bit])
    rows_pack = pown_ref.shape[0] // k

    def pack_box(e):
        ref = (pb_ref, pown_ref, pa_ref)[e // rows_pack]
        return box(ref, e % rows_pack)

    level1 = rows_pack - leaves

    def ext1_box(e):
        return pack_box((e // level1) * rows_pack + leaves + e % level1)

    def ext0_box(e):
        return pack_box((e // leaves) * rows_pack + e % leaves)

    b1 = []
    for j in range(2):
        gj = coupling(ext1_box, 2 * d - 2, j, lambda e, j=j: fpair_ref[j, e], 1)
        b1.append(gj + dot(expansion, ct_ref[2 + j]))
    for i in range(leaves):
        st = 2 * (i >> 1) + 2
        gi = coupling(lambda w, st=st: ext0_box(st + w), leaves * d + 2 * (i >> 1) - 2, i & 1,
                      lambda e, i=i: fleaf_ref[i, e], 0)
        b0 = gi + dot(b1[i >> 1], ct_ref[i & 1])
        far = jnp.dot(b0.astype(jnp.bfloat16), cb_ref[i], preferred_element_type=jnp.float32)
        near = spread_ref[reach + i]
        if i < reach:
            near = near + rb_ref[i]
        if i >= leaves - reach:
            near = near + ra_ref[i - (leaves - reach)]
        out_ref[:, pl.ds(i * width, width)] = far + near


def local(
    probes,
    row_basis,
    col_basis,
    near_blocks,
    near_cols,
    far_leaf,
    far_pair,
    far_top,
    row_transfer,
    col_transfer,
    coupling,
):
    leaves, basis_rank, leaf_width = row_basis.shape
    probe_count = probes.shape[0]
    near_reach = near_cols.shape[1] // 2
    levels_total = coupling.shape[0]
    devices = lax.axis_size(ALL)
    device = lax.axis_index(ALL)
    group_size = lax.axis_size(GROUP)
    in_group = lax.axis_index(GROUP)
    group = lax.axis_index("yz")
    groups = lax.axis_size("yz")
    all_leaves = devices * leaves
    first_leaf = device * leaves
    points = probes.reshape(probe_count, leaves, leaf_width)

    a0 = jnp.einsum("klp,lrp->lkr", points, row_basis, preferred_element_type=jnp.float32)
    a1 = halve(a0, row_transfer[0])
    a2 = halve(a1, row_transfer[1])

    grp = lax.all_gather(a2[0], GROUP, axis=0, tiled=False)
    up_levels = [grp]
    for height in range(2, 5):
        up_levels.append(halve(up_levels[-1], row_transfer[height]))

    products = jnp.einsum("klp,ljpq->ljkq", points, near_blocks, preferred_element_type=jnp.float32)
    span_width = leaves + 2 * near_reach
    targets = near_cols - (first_leaf - near_reach)
    places = jnp.arange(span_width, dtype=jnp.int32)
    scatter_table = (
        (targets[:, :, None] == places[None, None, :]) & (near_cols >= 0)[:, :, None]
    ).astype(jnp.float32)
    spread = jnp.einsum("lje,ljkq->ekq", scatter_table, products, precision=highest)
    rims = jnp.concatenate([spread[:near_reach], spread[span_width - near_reach :]], axis=0)
    rim_before, rim_after = padded(rims, ALL, near_reach)

    packed = jnp.concatenate([a0, a1], axis=0)
    pack_before, pack_after = padded(packed, ALL, packed.shape[0])

    starts = {}
    running = 0
    for height in range(2, levels_total):
        starts[height] = running
        running = running + (all_leaves >> height)

    gathered = lax.all_gather(up_levels[-1][0], "yz", axis=0, tiled=False)
    grp_before, grp_after = padded(grp, "yz", group_size)
    k, r = probe_count, basis_rank
    flat = lambda x: x.reshape(-1, r)
    n5 = gathered.shape[0]
    smem = pl.BlockSpec(memory_space=pltpu.SMEM)
    vmem = pl.BlockSpec(memory_space=pltpu.VMEM)
    out = pl.pallas_call(
        functools.partial(tree_kernel, starts=starts, k=k, r=r, leaves=leaves,
                          width=leaf_width, levels=levels_total, reach=near_reach),
        out_shape=jax.ShapeDtypeStruct((probe_count, leaves * leaf_width), jnp.float32),
        in_specs=[smem] * 4 + [vmem] * 14,
        out_specs=vmem,
        scratch_shapes=[pltpu.VMEM(((n5 >> i) * k + 4 * k, r), jnp.float32) for i in range(5)]
        + [pltpu.VMEM((3 * group_size * k, r), jnp.float32),
           pltpu.VMEM((12 * k, r), jnp.float32), pltpu.VMEM((6 * k, r), jnp.float32)],
    )(
        jnp.reshape(device, (1,)).astype(jnp.int32),
        far_top,
        far_leaf,
        far_pair,
        flat(gathered),
        flat(grp_before),
        flat(grp),
        flat(grp_after),
        flat(pack_before),
        flat(packed),
        flat(pack_after),
        row_transfer.reshape(-1, r, r),
        col_transfer.reshape(-1, r, r),
        coupling.reshape(-1, r, r),
        col_basis,
        spread,
        rim_before,
        rim_after,
    )
    return out


def solution(mesh):
    leaf_count, sub_count = mesh.devices.shape
    fine = Mesh(mesh.devices.reshape(leaf_count // 2, 2, sub_count), ALL)
    in_specs = (
        P(None, ALL),
        P(ALL, None, None),
        P(ALL, None, None),
        P(ALL, None, None, None),
        P(ALL, None),
        P(ALL, None),
        P(ALL, None),
        P(),
        P(),
        P(),
        P(),
    )
    out_specs = P(None, ALL)
    return jax.shard_map(local, mesh=fine, in_specs=in_specs, out_specs=out_specs, check_vma=False)
```

```python
import functools

import jax
import jax.numpy as jnp
from jax import lax
from jax.sharding import Mesh
from jax.experimental import pallas as pl
from jax.experimental.pallas import tpu as pltpu
from jax.sharding import PartitionSpec as P

highest = lax.Precision.HIGHEST
ALL = ("yz", "core", "sub")
GROUP = ("core", "sub")


def padded(shard, axis, width):
    devices, length = (lax.axis_size(axis), shard.shape[0])
    up = [(i, i + 1) for i in range(devices - 1)]
    down = [(j, i) for i, j in up]
    before = lax.ppermute(shard[length - width :], axis, up)
    after = lax.ppermute(shard[:width], axis, down)
    return before, after


def halve(coefficients, transfer):
    paired = coefficients.reshape(
        coefficients.shape[0] // 2, 2, coefficients.shape[1], coefficients.shape[2]
    )
    return jnp.einsum("bjkr,jrs->bks", paired, transfer, precision=highest)


def window_coupling(windows, bases, rows, odd, level_coupling):
    picks = (0, 1, 4, 5)
    stacked = jnp.concatenate([windows[:, w] for w in picks], axis=-1)
    hits = [
        jnp.any((rows == (bases + w)[:, None]) & (rows >= 0), axis=1) for w in picks
    ]
    even_cls = (1, 2, 4, 5)
    odd_cls = (0, 1, 3, 4)
    mats = []
    for i in range(4):
        chosen = jnp.where(
            odd[:, None, None], level_coupling[odd_cls[i]], level_coupling[even_cls[i]]
        )
        mats.append(jnp.where(hits[i][:, None, None], chosen, 0.0))
    matrix = jnp.concatenate(mats, axis=1)
    return jnp.einsum("bkr,brs->bks", stacked, matrix, precision=highest)


def one_box(level_array, offset, box, row, level_coupling):
    base = 2 * (box >> 1) - 2
    win = lax.dynamic_slice_in_dim(level_array, base - offset, 6, axis=0)
    return window_coupling(
        win[None], jnp.reshape(base, (1,)), row[None], jnp.reshape(box & 1, (1,)) == 1,
        level_coupling,
    )[0]


def tree_kernel(dev_ref, ftop_ref, fleaf_ref, fpair_ref, top5_ref, gb_ref, gown_ref, ga_ref,
                pb_ref, pown_ref, pa_ref, rt_ref, ct_ref, cp_ref, cb_ref, spread_ref, rb_ref, ra_ref,
                out_ref, p5, p6, p7, p8, p9, ext2_ref, e3, e4, *, starts, k, r, leaves, width, levels,
                reach):
    def dot(a, b):
        return jnp.dot(a, b, precision=lax.Precision.HIGH, preferred_element_type=jnp.float32)

    def halve_rows(x, n, height):
        v = x.reshape(n // 2, 2 * k, r)
        even = v[:, :k].reshape(n // 2 * k, r)
        odd = v[:, k:].reshape(n // 2 * k, r)
        return dot(even, rt_ref[2 * height]) + dot(odd, rt_ref[2 * height + 1])

    def box(ref, i):
        return ref[pl.ds(pl.multiple_of(i * k, k), k), :]

    def coupling(get, base, odd, row_at, level):
        total = jnp.zeros((k, r), jnp.float32)
        for w, cls in ((0, 1), (1, 2), (4, 4), (5, 5)):
            hit = jnp.int32(0)
            for j in range(4):
                e = row_at(j)
                hit = hit | ((e == base + w) & (e >= 0)).astype(jnp.int32)
            scale = hit.astype(jnp.float32)
            c = cls - odd
            total = total + dot(get(w) * scale, cp_ref[level * 6 + c])
        return total

    d = dev_ref[0]
    grp = d >> 3
    zeros2 = jnp.zeros((2 * k, r), jnp.float32)
    pads = [p5, p6, p7, p8, p9]
    x = top5_ref[...]
    n = x.shape[0] // k
    for idx, ref in enumerate(pads):
        ref[pl.ds(0, 2 * k), :] = zeros2
        ref[pl.ds((n + 2) * k, 2 * k), :] = zeros2
        ref[pl.ds(2 * k, n * k), :] = x
        if idx + 1 < len(pads):
            x = halve_rows(x, n, 5 + idx)
            n = n // 2
    span = gown_ref.shape[0]
    ext2_ref[pl.ds(0, span), :] = gb_ref[...]
    ext2_ref[pl.ds(span, span), :] = gown_ref[...]
    ext2_ref[pl.ds(2 * span, span), :] = ga_ref[...]
    e3[...] = halve_rows(ext2_ref[...], 24, 2)
    e4[...] = halve_rows(e3[...], 12, 3)

    g = {}
    for height in range(5, levels):
        t = grp >> (height - 5)
        base = 2 * (t >> 1) - 2
        row0 = starts[height] + t
        g[height] = coupling(lambda w, ref=pads[height - 5], st=base + 2: box(ref, st + w),
                             base, t & 1, lambda j, row=row0: ftop_ref[row, j], height)
    lg = d & 7
    mids = {2: (ext2_ref, 2 * (lg >> 1) + 6), 3: (e3, 2 * (lg >> 2) + 2), 4: (e4, 0)}
    for height in range(2, 5):
        t = d >> (height - 2)
        base = 2 * (t >> 1) - 2
        row0 = starts[height] + t
        ref, start = mids[height]
        g[height] = coupling(lambda w, ref=ref, st=start: box(ref, st + w),
                             base, t & 1, lambda j, row=row0: ftop_ref[row, j], height)
    expansion = g[levels - 1]
    for height in range(levels - 2, 1, -1):
        bit = (d >> (height - 2)) & 1
        expansion = g[height] + dot(expansion, ct_ref[2 * height + bit])
    rows_pack = pown_ref.shape[0] // k

    def pack_box(e):
        ref = (pb_ref, pown_ref, pa_ref)[e // rows_pack]
        return box(ref, e % rows_pack)

    level1 = rows_pack - leaves

    def ext1_box(e):
        return pack_box((e // level1) * rows_pack + leaves + e % level1)

    def ext0_box(e):
        return pack_box((e // leaves) * rows_pack + e % leaves)

    b1 = []
    for j in range(2):
        gj = coupling(ext1_box, 2 * d - 2, j, lambda e, j=j: fpair_ref[j, e], 1)
        b1.append(gj + dot(expansion, ct_ref[2 + j]))
    for i in range(leaves):
        st = 2 * (i >> 1) + 2
        gi = coupling(lambda w, st=st: ext0_box(st + w), leaves * d + 2 * (i >> 1) - 2, i & 1,
                      lambda e, i=i: fleaf_ref[i, e], 0)
        b0 = gi + dot(b1[i >> 1], ct_ref[i & 1])
        far = jnp.dot(b0.astype(jnp.bfloat16), cb_ref[i], preferred_element_type=jnp.float32)
        near = spread_ref[reach + i]
        if i < reach:
            near = near + rb_ref[i]
        if i >= leaves - reach:
            near = near + ra_ref[i - (leaves - reach)]
        out_ref[:, pl.ds(i * width, width)] = far + near


def local(
    probes,
    row_basis,
    col_basis,
    near_blocks,
    near_cols,
    far_leaf,
    far_pair,
    far_top,
    row_transfer,
    col_transfer,
    coupling,
):
    leaves, basis_rank, leaf_width = row_basis.shape
    probe_count = probes.shape[0]
    near_reach = near_cols.shape[1] // 2
    levels_total = coupling.shape[0]
    devices = lax.axis_size(ALL)
    device = lax.axis_index(ALL)
    group_size = lax.axis_size(GROUP)
    in_group = lax.axis_index(GROUP)
    group = lax.axis_index("yz")
    groups = lax.axis_size("yz")
    all_leaves = devices * leaves
    first_leaf = device * leaves
    points = probes.reshape(probe_count, leaves, leaf_width)

    a0 = jnp.einsum("klp,lrp->lkr", points, row_basis, preferred_element_type=jnp.float32)
    a1 = halve(a0, row_transfer[0])
    a2 = halve(a1, row_transfer[1])

    grp = lax.all_gather(a2[0], GROUP, axis=0, tiled=False)
    up_levels = [grp]
    for height in range(2, 5):
        up_levels.append(halve(up_levels[-1], row_transfer[height]))

    products = jnp.einsum("klp,ljpq->ljkq", points, near_blocks, preferred_element_type=jnp.float32)
    span_width = leaves + 2 * near_reach
    targets = near_cols - (first_leaf - near_reach)
    places = jnp.arange(span_width, dtype=jnp.int32)
    scatter_table = (
        (targets[:, :, None] == places[None, None, :]) & (near_cols >= 0)[:, :, None]
    ).astype(jnp.float32)
    spread = jnp.einsum("lje,ljkq->ekq", scatter_table, products, precision=highest)
    rims = jnp.concatenate([spread[:near_reach], spread[span_width - near_reach :]], axis=0)
    rim_before, rim_after = padded(rims, ALL, near_reach)

    packed = jnp.concatenate([a0, a1], axis=0)
    pack_before, pack_after = padded(packed, ALL, packed.shape[0])

    starts = {}
    running = 0
    for height in range(2, levels_total):
        starts[height] = running
        running = running + (all_leaves >> height)

    gathered = lax.all_gather(up_levels[-1][0], "yz", axis=0, tiled=False)
    grp_before, grp_after = padded(grp, "yz", group_size)
    k, r = probe_count, basis_rank
    flat = lambda x: x.reshape(-1, r)
    n5 = gathered.shape[0]
    smem = pl.BlockSpec(memory_space=pltpu.SMEM)
    vmem = pl.BlockSpec(memory_space=pltpu.VMEM)
    out = pl.pallas_call(
        functools.partial(tree_kernel, starts=starts, k=k, r=r, leaves=leaves,
                          width=leaf_width, levels=levels_total, reach=near_reach),
        out_shape=jax.ShapeDtypeStruct((probe_count, leaves * leaf_width), jnp.float32),
        in_specs=[smem] * 4 + [vmem] * 14,
        out_specs=vmem,
        scratch_shapes=[pltpu.VMEM(((n5 >> i) * k + 4 * k, r), jnp.float32) for i in range(5)]
        + [pltpu.VMEM((3 * group_size * k, r), jnp.float32),
           pltpu.VMEM((12 * k, r), jnp.float32), pltpu.VMEM((6 * k, r), jnp.float32)],
    )(
        jnp.reshape(device, (1,)).astype(jnp.int32),
        far_top,
        far_leaf,
        far_pair,
        flat(gathered),
        flat(grp_before),
        flat(grp),
        flat(grp_after),
        flat(pack_before),
        flat(packed),
        flat(pack_after),
        row_transfer.reshape(-1, r, r),
        col_transfer.reshape(-1, r, r),
        coupling.reshape(-1, r, r),
        col_basis,
        spread,
        rim_before,
        rim_after,
    )
    return out


def solution(mesh):
    leaf_count, sub_count = mesh.devices.shape
    fine = Mesh(mesh.devices.reshape(leaf_count // 2, 2, sub_count), ALL)
    in_specs = (
        P(None, ALL),
        P(ALL, None, None),
        P(ALL, None, None),
        P(ALL, None, None, None),
        P(ALL, None),
        P(ALL, None),
        P(ALL, None),
        P(),
        P(),
        P(),
        P(),
    )
    out_specs = P(None, ALL)
    return jax.shard_map(local, mesh=fine, in_specs=in_specs, out_specs=out_specs, check_vma=False)
```
